512 devices in a mesh: row: 32 (over z_hi, x, core), col: 16 (over z_lo, y).
Axes of the slice: x: 4, y: 8, z: 8 (z_hi: 4, z_lo: 2; z = z_hi * 2 + z_lo), core: 2. Of those that a mesh axis runs over, the one named last changes fastest.
Arguments:
- amps: float32 [32, 4, 576, 576], P(None, None, 'row', 'col'), may hold values from -6 to 6
- integrals: float32 [4, 576, 32, 576], P(None, 'row', 'col'), may hold values from -0.5 to 0.5
- e_occ: float32 [32], replicated, may hold values from -2 to -0.5
- e_vir: float32 [576], replicated, may hold values from 0.5 to 3
Outputs:
- update: float32 [32, 32, 576, 576], P('row', 'col')
The draws below stay inside these ranges and needn't reach their ends.
All inputs are finite; a program needn't handle non-finite values.
Results may differ from the reference program's by a relative error of at most 0.00007.
Values sent between devices are 32-bit elements; how exact they have to be, the bound alone decides.
No kernel may reach another device: no remote copies, remote signals or barrier semaphores. Data moves between devices by JAX's collectives and lax.ppermute only.
A program may use at most 128 MiB of HBM per device.

```python
import jax
import jax.numpy as jnp
from jax import lax

O = 32
V = 576
KW = 4


def steps_of(rng, dims, shards, least, top_value):
    factor_of, own = 1.0, jax.random.fold_in(rng, 6)
    for position, blocks in shards:
        heights = jnp.exp(jax.random.uniform(jax.random.fold_in(own, position), (blocks,), jnp.float32, least / len(shards), top_value / len(shards)))
        factor_of = factor_of * jnp.repeat(heights, dims[position] // blocks).reshape([-1 if axis == position else 1 for axis in range(len(dims))])
    return factor_of


def bell_draw(rng, extent, deviation, bound, pieces=(), kind=jnp.bfloat16):
    level = steps_of(rng, extent, pieces, -0.22, 0.18) if pieces else 1.0
    values = jax.random.normal(rng, extent, jnp.float32) * deviation * level
    return jnp.minimum(jnp.maximum(values, -bound), bound).astype(kind)


def setup_inputs(seed: int = 0) -> dict:
    streams_of = jax.random.split(jax.random.key(seed), 5)
    amps = bell_draw(streams_of[0], (O, KW, V, V), 1.0, 6.0, ((2, 32), (3, 16)), jnp.float32)
    integrals = bell_draw(streams_of[1], (KW, V, O, V), (KW * V // 16) ** -0.5, 0.5, ((1, 32), (2, 16)), jnp.float32)
    e_occ = jnp.clip(jax.random.uniform(streams_of[2], (O,), jnp.float32, -2.0, -0.5), -2.0, -0.5)
    e_vir = jnp.clip(jax.random.uniform(streams_of[3], (V,), jnp.float32, 0.5, 3.0), 0.5, 3.0)
    return dict(amps=amps, integrals=integrals, e_occ=e_occ, e_vir=e_vir)


def reference(amps, integrals, e_occ, e_vir):
    def one_index(pair):
        amp_block, energy = pair
        contracted = jnp.einsum("kac,kcjb->jab", amp_block.astype(jnp.float32), integrals.astype(jnp.float32), precision=lax.Precision.HIGHEST)
        denom = energy + e_occ[:, None, None] - e_vir[None, :, None] - e_vir[None, None, :]
        return contracted / denom

    return lax.map(one_index, (amps, e_occ))
```

```python
import jax
import jax.numpy as jnp
from jax import lax
from jax.sharding import Mesh, PartitionSpec as P

ROWS = ("chip", "core")


def contract(left, right):
    return jnp.einsum(
        "ikac,kcjb->ijab",
        left,
        right,
        precision=lax.Precision.HIGHEST,
        preferred_element_type=jnp.float32,
    )


def shards(amps, integrals, e_occ, e_vir):
    n_chip = lax.axis_size("chip")
    n_core = lax.axis_size("core")
    chip = lax.axis_index("chip")
    core = lax.axis_index("core")
    col = lax.axis_index("col")
    occ, kw, va, vc = amps.shape
    _, vr, jc, nb = integrals.shape
    kh = kw // n_core
    ipc = occ // (n_chip * n_core) * n_core
    t = amps.reshape(n_chip, ipc, n_core, kh, va, vc).transpose(0, 2, 1, 3, 4, 5)
    t = t.reshape(n_chip * n_core, ipc, kh, va, vc)
    t = lax.all_to_all(t, ROWS, 0, 0, tiled=True)
    t = t.transpose(1, 2, 0, 3, 4).reshape(ipc, kh, -1, vc)
    t = lax.all_gather(t, "col", axis=3, tiled=True)
    g = integrals.reshape(n_core, kh, vr, jc, nb)
    g = lax.all_to_all(g, "core", 0, 0, tiled=True)
    g = g.transpose(1, 0, 2, 3, 4).reshape(kh, n_core * vr, jc, nb)
    g = lax.all_gather(g, "chip", axis=1, tiled=True)
    part = contract(t, g)
    part = lax.all_to_all(part, "core", 0, 0, tiled=True)
    contracted = part[0] + part[1]
    i_energy = lax.dynamic_slice_in_dim(e_occ, chip * n_core + core, 1)
    j_energy = lax.dynamic_slice_in_dim(e_occ, col * jc, jc)
    denom = (
        i_energy[:, None, None, None]
        + j_energy[None, :, None, None]
        - e_vir[None, None, :, None]
        - e_vir[None, None, None, :]
    )
    return contracted[None] / denom


def solution(mesh):
    rows = mesh.shape["row"]
    cols = mesh.shape["col"]
    split = Mesh(mesh.devices.reshape(rows // 2, 2, cols), ("chip", "core", "col"))
    placed = (P(None, None, ROWS, "col"), P(None, ROWS, "col", None), P(), P())
    return jax.shard_map(
        shards, mesh=split, in_specs=placed, out_specs=P(ROWS, "col", None, None), check_vma=False
    )
```

```python
import jax
import jax.numpy as jnp
from jax import lax
from jax.sharding import Mesh, PartitionSpec as P

CHIP = ("zh", "x")
ROWS = ("zh", "x", "core")
COLS = ("zl", "y")


def contract(left, right):
    return jnp.einsum(
        "yzikac,kzycjb->ijab",
        left,
        right,
        precision=lax.Precision.HIGHEST,
        preferred_element_type=jnp.float32,
    )


def ring_y(x):
    n = lax.axis_size("y")
    me = lax.axis_index("y")
    right = [(d, (d + 1) % n) for d in range(n)]
    left = [(d, (d - 1) % n) for d in range(n)]
    by_offset = [None] * n
    by_offset[0] = x
    from_left = from_right = x
    for step in range(1, n // 2 + 1):
        from_left = lax.ppermute(from_left, "y", right)
        by_offset[(-step) % n] = from_left
        if step < n - step:
            from_right = lax.ppermute(from_right, "y", left)
            by_offset[step] = from_right
    stacked = jnp.stack(by_offset)
    doubled = jnp.concatenate([stacked, stacked])
    return lax.dynamic_slice_in_dim(doubled, (n - me) % n, n)


def shards(amps, integrals, e_occ, e_vir):
    n_chip = lax.axis_size(CHIP)
    n_core = lax.axis_size("core")
    n_zl = lax.axis_size("zl")
    row = lax.axis_index(ROWS)
    col = lax.axis_index(COLS)
    occ, kw, va, vc = amps.shape
    _, vr, jc, nb = integrals.shape
    kh = kw // n_core
    ipc = occ // n_chip
    t = amps.reshape(n_chip, ipc, n_core, kh, va, vc).transpose(0, 2, 1, 3, 4, 5)
    t = t.reshape(n_chip * n_core, ipc, kh, va, vc)
    t = lax.all_to_all(t, ROWS, 0, 0, tiled=True)
    t = t.transpose(1, 2, 0, 3, 4).reshape(ipc, kh, -1, vc)
    other = lax.ppermute(t, "zl", [(0, 1), (1, 0)])
    first = lax.axis_index("zl") == 0
    t = jnp.stack([jnp.where(first, t, other), jnp.where(first, other, t)])
    t = ring_y(t)
    g = integrals.reshape(n_core, kh, vr, jc, nb)
    g = lax.all_to_all(g, "core", 0, 0, tiled=True)
    g = g.transpose(1, 0, 2, 3, 4).reshape(kh, n_core * vr, jc, nb)
    g = lax.all_gather(g, CHIP, axis=1, tiled=True)
    g = g.reshape(kh, n_zl, lax.axis_size("y"), vc, jc, nb)
    part = contract(t, g)
    part = lax.all_to_all(part, "core", 0, 0, tiled=True)
    contracted = part[0] + part[1]
    i_energy = lax.dynamic_slice_in_dim(e_occ, row, 1)
    j_energy = lax.dynamic_slice_in_dim(e_occ, col * jc, jc)
    denom = (
        i_energy[:, None, None, None]
        + j_energy[None, :, None, None]
        - e_vir[None, None, :, None]
        - e_vir[None, None, None, :]
    )
    return contracted[None] / denom


def solution(mesh):
    devices = mesh.devices.reshape(4, mesh.shape["row"] // 8, 2, 2, mesh.shape["col"] // 2)
    split = Mesh(devices, ("zh", "x", "core", "zl", "y"))
    placed = (P(None, None, ROWS, COLS), P(None, ROWS, COLS, None), P(), P())
    return jax.shard_map(
        shards, mesh=split, in_specs=placed, out_specs=P(ROWS, COLS, None, None), check_vma=False
    )
```

```python
import jax
import jax.numpy as jnp
from jax import lax
from jax.sharding import Mesh, PartitionSpec as P

CHIP = ("zh", "x")
ROWS = ("zh", "x", "core")
COLS = ("zl", "y")


def contract(left, right):
    return jnp.einsum(
        "yzikac,kzycjb->ijab",
        left,
        right,
        precision=lax.Precision.HIGH,
        preferred_element_type=jnp.float32,
    )


def ring_y(x):
    n = lax.axis_size("y")
    me = lax.axis_index("y")
    right = [(d, (d + 1) % n) for d in range(n)]
    left = [(d, (d - 1) % n) for d in range(n)]
    by_offset = [None] * n
    by_offset[0] = x
    from_left = from_right = x
    for step in range(1, n // 2 + 1):
        from_left = lax.ppermute(from_left, "y", right)
        by_offset[(-step) % n] = from_left
        if step < n - step:
            from_right = lax.ppermute(from_right, "y", left)
            by_offset[step] = from_right
    return jnp.stack(by_offset)


def shards(amps, integrals, e_occ, e_vir):
    n_chip = lax.axis_size(CHIP)
    n_core = lax.axis_size("core")
    n_zl = lax.axis_size("zl")
    row = lax.axis_index(ROWS)
    col = lax.axis_index(COLS)
    occ, kw, va, vc = amps.shape
    _, vr, jc, nb = integrals.shape
    kh = kw // n_core
    ipc = occ // n_chip
    t = amps.reshape(n_chip, ipc, n_core, kh, va, vc).transpose(0, 2, 1, 3, 4, 5)
    t = t.reshape(n_chip * n_core, ipc, kh, va, vc)
    t = lax.all_to_all(t, ROWS, 0, 0, tiled=True)
    t = t.transpose(1, 2, 0, 3, 4).reshape(ipc, kh, -1, vc)
    t, integrals = lax.optimization_barrier((t, integrals))
    other = lax.ppermute(t, "zl", [(0, 1), (1, 0)])
    first = lax.axis_index("zl") == 0
    t = jnp.stack([jnp.where(first, t, other), jnp.where(first, other, t)])
    t = ring_y(t)
    g = integrals.reshape(n_core, kh, vr, jc, nb)
    g = lax.all_to_all(g, "core", 0, 0, tiled=True)
    g = g.transpose(1, 0, 2, 3, 4).reshape(kh, n_core * vr, jc, nb)
    g = lax.all_gather(g, CHIP, axis=1, tiled=True)
    n_y = lax.axis_size("y")
    g = g.reshape(kh, n_zl, n_y, vc, jc, nb)
    g = jnp.concatenate([g, g], axis=2)
    g = lax.dynamic_slice_in_dim(g, lax.axis_index("y"), n_y, axis=2)
    part = contract(t, g)
    part = lax.all_to_all(part, "core", 0, 0, tiled=True)
    contracted = part[0] + part[1]
    i_energy = lax.dynamic_slice_in_dim(e_occ, row, 1)
    j_energy = lax.dynamic_slice_in_dim(e_occ, col * jc, jc)
    denom = (
        i_energy[:, None, None, None]
        + j_energy[None, :, None, None]
        - e_vir[None, None, :, None]
        - e_vir[None, None, None, :]
    )
    return contracted[None] / denom


def solution(mesh):
    devices = mesh.devices.reshape(4, mesh.shape["row"] // 8, 2, 2, mesh.shape["col"] // 2)
    split = Mesh(devices, ("zh", "x", "core", "zl", "y"))
    placed = (P(None, None, ROWS, COLS), P(None, ROWS, COLS, None), P(), P())
    return jax.shard_map(
        shards, mesh=split, in_specs=placed, out_specs=P(ROWS, COLS, None, None), check_vma=False
    )
```
